1024 devices in a mesh: ctx: 64 (over x, y, z_hi, core), fsdp: 16 (over z_lo).
Axes of the slice: x: 4, y: 4, z: 32 (z_hi: 2, z_lo: 16; z = z_hi * 16 + z_lo), core: 2. Of those that a mesh axis runs over, the one named last changes fastest.
Arguments:
- hidden: bfloat16 [2, 16, 4096, 3584], P(None, 'fsdp', 'ctx'), may hold values from -6 to 6
- queries: bfloat16 [2, 16, 4096, 1792], P(None, 'fsdp', 'ctx'), may hold values from -180 to 180
- kv_panel: bfloat16 [2, 3584, 256], P(None, 'fsdp'), may hold values from -0.09375 to 0.09375
- layout: int32 [16, 64], P('fsdp'), may hold values from 0 to 63, each once within a row
Outputs:
- attended: bfloat16 [2, 16, 4096, 1792], P(None, 'fsdp', 'ctx')
The draws below stay inside these ranges and needn't reach their ends.
Inputs may be any that keep to these rules, and one draw needn't show every extreme that they name: `layout`: each row names every block number of a sequence once.
All inputs are finite; a program needn't handle non-finite values.
Results may differ from the reference program's by a relative error of at most 0.02.
The reference program's roundings to bfloat16 on the way count: a program that leaves them out, or rounds other values in their place, can miss the bound.
Values may be sent and summed in bfloat16 or wider, within the bound.
No kernel may reach another device: no remote copies, remote signals or barrier semaphores. Data moves between devices by JAX's collectives and lax.ppermute only.
A program may use at most 32 MiB of HBM per device.

```python
import math
import jax
import jax.numpy as jnp
from jax import lax

D = 3584
HD = 128
QPK = 7
KVH = 2
BLK = 64
QH = 14
NBLK = 64
SEQ = 4096
SEQS = 16


def draw_queries(key, part):
    key_base = jax.random.fold_in(key, 0)
    full_shape = (2, SEQS, SEQ, QH * HD)
    return jnp.clip(jax.random.normal(key_base, full_shape, jnp.float32), -4.0, 4.0).astype(jnp.bfloat16)


def shard_levels(rng, dims, cuts, smallest, largest):
    gain = 1.0
    for axis_at, parts in cuts:
        heights = jax.random.uniform(jax.random.fold_in(jax.random.fold_in(rng, 6), axis_at), (parts,), jnp.float32, smallest / len(cuts), largest / len(cuts))
        gain = gain * jnp.repeat(jnp.exp(heights), dims[axis_at] // parts).reshape((-1,) + (1,) * (len(dims) - 1 - axis_at))
    return gain


def scatter_about(stream_key, extent, width, reach, shards=(), held_as=jnp.bfloat16):
    entries = jax.random.normal(stream_key, extent, jnp.float32) * width
    if len(shards) > 0:
        entries = shard_levels(stream_key, extent, shards, -0.22, 0.18) * entries
    return jnp.clip(entries, min=-reach, max=reach).astype(held_as)


def setup_inputs(seed: int = 0) -> dict:
    keys = jax.random.split(jax.random.key(seed), 5)
    hidden = scatter_about(keys[0], (2, SEQS, SEQ, D), 1.0, 6.0, ((1, 16), (2, 64)))
    queries = draw_queries(jax.random.fold_in(keys[4], 71), 0)
    kv_panel = scatter_about(keys[2], (KVH, D, 2 * HD), D ** -0.5, 0.09375, ((1, 16),))
    layout = jax.vmap(lambda own: jax.random.permutation(own, NBLK))(jax.random.split(keys[3], SEQS)).reshape((SEQS, NBLK)).astype(jnp.int32)
    return dict(hidden=hidden, queries=queries, kv_panel=kv_panel, layout=layout)


def rotate_keys(vectors_in, positions, head_dim):
    half_dim = head_dim // 2
    inverse = 1000000.0 ** (-(jnp.arange(half_dim, dtype=jnp.float32) * 2.0 / head_dim))
    angles = positions.astype(jnp.float32)[:, None] * inverse[None, :]
    cosine = jnp.cos(angles)[:, None, :]
    sine_part = jnp.sin(angles)[:, None, :]
    first_half = vectors_in[..., :half_dim]
    second_half = vectors_in[..., half_dim:]
    return jnp.concatenate([first_half * cosine - second_half * sine_part, second_half * cosine + first_half * sine_part], axis=-1)


def reference(hidden, queries, kv_panel, layout):
    panel_flat = jnp.transpose(kv_panel, (1, 0, 2)).reshape(D, KVH * 2 * HD)
    query_width = QH * HD
    q_block = math.gcd(SEQ, 256)
    score_scale = HD ** -0.5
    kind_shift = jnp.array([1, 0], dtype=jnp.int32)

    def one_sequence(packed):
        states, vectors, block_order = packed
        projected = jnp.dot(states.reshape(2 * SEQ, D), panel_flat, preferred_element_type=jnp.float32).reshape(2, SEQ, KVH, 2 * HD)
        block_of = jnp.repeat(block_order.astype(jnp.int32), BLK)
        positions = block_of * BLK + jnp.tile(jnp.arange(BLK, dtype=jnp.int32), NBLK)
        key_rows = rotate_keys(projected[..., :HD], positions, HD).astype(jnp.bfloat16)
        value_rows = projected[..., HD:].astype(jnp.bfloat16)

        def one_block(first_row):
            first_row = first_row.astype(jnp.int32)
            query_rows = lax.dynamic_slice_in_dim(vectors, first_row, q_block, 1).reshape(2, q_block, KVH, QPK, HD).astype(jnp.float32)
            key_all = jnp.concatenate([key_rows[0], lax.dynamic_slice_in_dim(key_rows[1], first_row, q_block, 0)], axis=0).astype(jnp.float32)
            value_all = jnp.concatenate([value_rows[0], lax.dynamic_slice_in_dim(value_rows[1], first_row, q_block, 0)], axis=0).astype(jnp.float32)
            query_block_of = lax.dynamic_slice_in_dim(block_of, first_row, q_block, 0)
            clean_ok = block_of[None, None, :] < query_block_of[None, :, None] + kind_shift[:, None, None]
            noisy_ok = (query_block_of[:, None] == query_block_of[None, :])[None] & (kind_shift[:, None, None] == 0)
            allowed = jnp.concatenate([clean_ok, noisy_ok], axis=-1)[:, None, None]
            scores = jnp.einsum('ctgpd,ugd->cgptu', query_rows, key_all) * score_scale
            scores = jnp.where(allowed, scores, -1e30)
            row_max = jnp.max(scores, axis=-1)
            weights = jnp.where(allowed, jnp.exp(scores - row_max[..., None]), 0.0)
            denominator = jnp.sum(weights, axis=-1)
            rounded = lax.optimization_barrier(weights.astype(jnp.bfloat16)).astype(jnp.float32)
            mixed = jnp.einsum('cgptu,ugd->cgptd', rounded, value_all) / denominator[..., None]
            return jnp.transpose(mixed, (0, 3, 1, 2, 4)).reshape(2, q_block, query_width).astype(jnp.bfloat16)

        block_starts = jnp.arange(SEQ // q_block, dtype=jnp.int32) * q_block
        blocks = lax.map(one_block, block_starts)
        return jnp.transpose(blocks, (1, 0, 2, 3)).reshape(2, SEQ, query_width)

    result = lax.map(one_sequence, (jnp.transpose(hidden, (1, 0, 2, 3)), jnp.transpose(queries, (1, 0, 2, 3)), layout))
    return jnp.transpose(result, (1, 0, 2, 3))
```

```python
import math

import jax
import jax.numpy as jnp
from jax import lax
from jax.sharding import Mesh
from jax.sharding import PartitionSpec as P

NEGATIVE = -1e30
CTX = ("x", "y", "zh", "core")


def rotate_keys(vectors_in, positions, head_dim):
    half_dim = head_dim // 2
    inverse = 1000000.0 ** (-(jnp.arange(half_dim, dtype=jnp.float32) * 2.0 / head_dim))
    angles = positions.astype(jnp.float32)[..., None] * inverse
    cosine = jnp.cos(angles)
    sine_part = jnp.sin(angles)
    first_half = vectors_in[..., :half_dim]
    second_half = vectors_in[..., half_dim:]
    return jnp.concatenate(
        [
            first_half * cosine - second_half * sine_part,
            second_half * cosine + first_half * sine_part,
        ],
        axis=-1,
    )


def absorb(fold_carry, query_rows, key_part, value_part, allowed, score_scale):
    running, denominator, numerator = fold_carry
    scores = (
        jnp.einsum("tpd,ud->ptu", query_rows, key_part, preferred_element_type=jnp.float32)
        * score_scale
    )
    allowed_all = allowed[None]
    scores = jnp.where(allowed_all, scores, NEGATIVE)
    highest = jnp.maximum(running, jnp.max(scores, axis=-1))
    factor = jnp.exp(running - highest)
    weights = jnp.where(allowed_all, jnp.exp(scores - highest[..., None]), 0.0)
    denominator = denominator * factor + jnp.sum(weights, axis=-1)
    numerator = numerator * factor[..., None] + jnp.einsum(
        "ptu,ud->ptd",
        weights.astype(jnp.bfloat16),
        value_part,
        preferred_element_type=jnp.float32,
    )
    return (highest, denominator, numerator)


def absorb_tiled(fold_carry, query_rows, key_part, value_part, allowed, score_scale):
    key_count = key_part.shape[0]
    tile_width = math.gcd(key_count, 512)

    def one_tile(tile_index, inner):
        tile_start = tile_index * tile_width
        return absorb(
            inner,
            query_rows,
            lax.dynamic_slice_in_dim(key_part, tile_start, tile_width, 0),
            lax.dynamic_slice_in_dim(value_part, tile_start, tile_width, 0),
            lax.dynamic_slice_in_dim(allowed, tile_start, tile_width, 1),
            score_scale,
        )

    return lax.fori_loop(0, key_count // tile_width, one_tile, fold_carry)


def attend_block(query_rows, noisy_keys, noisy_values, clean_keys, clean_values, key_blocks,
                 own_block, block_len, score_scale):
    group_size = query_rows.shape[1]
    head_dim = query_rows.shape[2]
    rows_all = 2 * block_len
    fold_carry = (
        jnp.full((group_size, rows_all), NEGATIVE, jnp.float32),
        jnp.zeros((group_size, rows_all), jnp.float32),
        jnp.zeros((group_size, rows_all, head_dim), jnp.float32),
    )
    noisy_ok = jnp.broadcast_to((jnp.arange(rows_all) >= block_len)[:, None], (rows_all, block_len))
    fold_carry = absorb(fold_carry, query_rows, noisy_keys, noisy_values, noisy_ok, score_scale)
    block_limit = (
        jnp.concatenate([jnp.ones((block_len,), jnp.int32), jnp.zeros((block_len,), jnp.int32)])
        + own_block
    )
    key_block = jnp.repeat(key_blocks, block_len)
    allowed = key_block[None, :] < block_limit[:, None]
    fold_carry = absorb_tiled(fold_carry, query_rows, clean_keys, clean_values, allowed, score_scale)
    highest, denominator, numerator = fold_carry
    return jnp.transpose(numerator / denominator[..., None], (1, 0, 2))


def swap(value, axis):
    return lax.ppermute(value, axis, [(0, 1), (1, 0)])


def ring4(value, axis):
    size = 4
    forward = [(i, (i + 1) % size) for i in range(size)]
    backward = [(i, (i - 1) % size) for i in range(size)]
    from_left = lax.ppermute(value, axis, forward)
    from_right = lax.ppermute(value, axis, backward)
    from_left2 = lax.ppermute(from_left, axis, forward)
    return jnp.stack([value, from_left, from_left2, from_right])


RING_SHIFT = (0, -1, -2, 1)


def local(hidden, queries, kv_panel, layout):
    block_len = hidden.shape[2]
    model_width = hidden.shape[3]
    heads_kv = kv_panel.shape[0]
    chunk_rows = kv_panel.shape[1]
    head_dim = kv_panel.shape[2] // 2
    group_size = queries.shape[3] // (heads_kv * head_dim)
    group_width = group_size * head_dim
    score_scale = head_dim ** (-0.5)
    n_chunks = model_width // chunk_rows
    x = lax.axis_index("x")
    y = lax.axis_index("y")
    zh = lax.axis_index("zh")
    core = lax.axis_index("core")
    fsdp = lax.axis_index("fsdp")
    ctx = ((x * 4 + y) * 2 + zh) * 2 + core
    block_table = layout[0]

    z_size = 2 * n_chunks
    forward = [(z, (z + 1) % z_size) for z in range(z_size)]
    backward = [(z, (z - 1) % z_size) for z in range(z_size)]
    mine = lax.dynamic_index_in_dim(kv_panel, core, 0, keepdims=False)
    panel = jnp.zeros((n_chunks,) + mine.shape, mine.dtype)
    panel = lax.dynamic_update_index_in_dim(panel, mine, fsdp, 0)
    going_up = mine
    going_down = mine
    for step in range(1, n_chunks // 2 + 1):
        going_up = lax.ppermute(going_up, ("zh", "fsdp"), forward)
        panel = lax.dynamic_update_index_in_dim(panel, going_up, (fsdp - step) % n_chunks, 0)
        if step < n_chunks // 2:
            going_down = lax.ppermute(going_down, ("zh", "fsdp"), backward)
            panel = lax.dynamic_update_index_in_dim(
                panel, going_down, (fsdp + step) % n_chunks, 0
            )
    panel = panel.reshape(model_width, 2 * head_dim)

    own_rows = hidden.reshape(2, block_len, model_width)
    token_rows = jnp.stack([own_rows, swap(own_rows, "core")])
    own_queries = queries.reshape(2, block_len, heads_kv, group_width)
    query_mine = lax.dynamic_index_in_dim(own_queries, core, 2, keepdims=False)
    query_other = lax.dynamic_index_in_dim(own_queries, 1 - core, 2, keepdims=False)
    query_blocks = jnp.stack([query_mine, swap(query_other, "core")])
    ctx_blocks = jnp.stack([ctx, ctx + 1 - 2 * core])
    own_blocks = block_table[ctx_blocks]

    projected = jnp.einsum(
        "bctd,de->bcte", token_rows, panel, preferred_element_type=jnp.float32
    )
    positions = own_blocks[:, None] * block_len + jnp.arange(block_len, dtype=jnp.int32)
    key_rows = rotate_keys(projected[..., :head_dim], positions[:, None, :], head_dim).astype(
        jnp.bfloat16
    )
    value_rows = projected[..., head_dim:].astype(jnp.bfloat16)

    clean = jnp.concatenate([key_rows[:, 0], value_rows[:, 0]], axis=-1)
    gathered = jnp.stack([clean, swap(clean, "zh")])
    gathered = ring4(gathered, "x")
    gathered = ring4(gathered, "y")
    gathered = gathered.reshape(-1, 2 * head_dim)
    shifts = jnp.array(RING_SHIFT, jnp.int32)
    src_y = (y + shifts)[:, None, None, None] % 4
    src_x = (x + shifts)[None, :, None, None] % 4
    src_zh = (zh + jnp.arange(2))[None, None, :, None] % 2
    src_core = (core + jnp.arange(2))[None, None, None, :] % 2
    src = ((src_x * 4 + src_y) * 2 + src_zh) * 2 + src_core
    key_blocks = block_table[src.reshape(-1)]
    clean_keys = gathered[:, :head_dim]
    clean_values = gathered[:, head_dim:]

    query_rows = query_blocks.reshape(2, 2 * block_len, group_size, head_dim)
    attended = jax.vmap(
        lambda q, nk, nv, b: attend_block(
            q, nk, nv, clean_keys, clean_values, key_blocks, b, block_len, score_scale
        )
    )(query_rows, key_rows[:, 1], value_rows[:, 1], own_blocks)
    attended = attended.astype(jnp.bfloat16).reshape(2, 2, block_len, group_width)
    returned = swap(attended[1], "core")
    first = jnp.where(core == 0, attended[0], returned)
    second = jnp.where(core == 0, returned, attended[0])
    result = jnp.concatenate([first, second], axis=-1)
    return result.reshape(2, 1, block_len, heads_kv * group_width)


def solution(mesh):
    axis_sizes = dict(zip(mesh.axis_names, mesh.devices.shape))
    assert axis_sizes["ctx"] == 64
    fine = Mesh(mesh.devices.reshape(4, 4, 2, 2, axis_sizes["fsdp"]), CTX + ("fsdp",))
    return jax.shard_map(
        local,
        mesh=fine,
        in_specs=(
            P(None, "fsdp", CTX, None),
            P(None, "fsdp", CTX, None),
            P(None, "fsdp", None),
            P("fsdp", None),
        ),
        out_specs=P(None, "fsdp", CTX, None),
        check_vma=False,
    )
```

```python
import math

import jax
import jax.numpy as jnp
from jax import lax
from jax.sharding import Mesh
from jax.sharding import PartitionSpec as P

NEGATIVE = -1e30
CTX = ("x", "y", "zh", "core")


def rotate_keys(vectors_in, positions, head_dim):
    half_dim = head_dim // 2
    inverse = 1000000.0 ** (-(jnp.arange(half_dim, dtype=jnp.float32) * 2.0 / head_dim))
    angles = positions.astype(jnp.float32)[..., None] * inverse
    cosine = jnp.cos(angles)
    sine_part = jnp.sin(angles)
    first_half = vectors_in[..., :half_dim]
    second_half = vectors_in[..., half_dim:]
    return jnp.concatenate(
        [
            first_half * cosine - second_half * sine_part,
            second_half * cosine + first_half * sine_part,
        ],
        axis=-1,
    )


def absorb(fold_carry, query_rows, key_part, value_part, allowed, score_scale):
    running, denominator, numerator = fold_carry
    scores = (
        jnp.einsum("tpd,ud->ptu", query_rows, key_part, preferred_element_type=jnp.float32)
        * score_scale
    )
    allowed_all = allowed[None]
    scores = jnp.where(allowed_all, scores, NEGATIVE)
    highest = jnp.maximum(running, jnp.max(scores, axis=-1))
    factor = jnp.exp(running - highest)
    weights = jnp.where(allowed_all, jnp.exp(scores - highest[..., None]), 0.0)
    denominator = denominator * factor + jnp.sum(weights, axis=-1)
    numerator = numerator * factor[..., None] + jnp.einsum(
        "ptu,ud->ptd",
        weights.astype(jnp.bfloat16),
        value_part,
        preferred_element_type=jnp.float32,
    )
    return (highest, denominator, numerator)


def absorb_tiled(fold_carry, query_rows, key_part, value_part, allowed, score_scale):
    key_count = key_part.shape[0]
    tile_width = math.gcd(key_count, 512)

    def one_tile(tile_index, inner):
        tile_start = tile_index * tile_width
        return absorb(
            inner,
            query_rows,
            lax.dynamic_slice_in_dim(key_part, tile_start, tile_width, 0),
            lax.dynamic_slice_in_dim(value_part, tile_start, tile_width, 0),
            lax.dynamic_slice_in_dim(allowed, tile_start, tile_width, 1),
            score_scale,
        )

    return lax.fori_loop(0, key_count // tile_width, one_tile, fold_carry)


def empty_state(blocks, group_size, rows_all, head_dim):
    return (
        jnp.full((blocks, group_size, rows_all), NEGATIVE, jnp.float32),
        jnp.zeros((blocks, group_size, rows_all), jnp.float32),
        jnp.zeros((blocks, group_size, rows_all, head_dim), jnp.float32),
    )


def absorb_chunk(fold_carry, query_rows, chunk, key_blocks, row_limit, score_scale):
    head_dim = query_rows.shape[-1]
    block_len = chunk.shape[-2]
    chunk = chunk.reshape(-1, 2 * head_dim)
    key_block = jnp.repeat(key_blocks.reshape(-1), block_len)
    allowed = key_block[None, None, :] < row_limit[:, :, None]
    return jax.vmap(absorb, in_axes=(0, 0, None, None, 0, None))(
        fold_carry, query_rows, chunk[:, :head_dim], chunk[:, head_dim:], allowed, score_scale
    )


def merge(first, second):
    high_a, den_a, num_a = first
    high_b, den_b, num_b = second
    highest = jnp.maximum(high_a, high_b)
    factor_a = jnp.exp(high_a - highest)
    factor_b = jnp.exp(high_b - highest)
    return (
        highest,
        den_a * factor_a + den_b * factor_b,
        num_a * factor_a[..., None] + num_b * factor_b[..., None],
    )


def swap(value, axis):
    return lax.ppermute(value, axis, [(0, 1), (1, 0)])


def ring4(value, axis):
    size = 4
    forward = [(i, (i + 1) % size) for i in range(size)]
    backward = [(i, (i - 1) % size) for i in range(size)]
    from_left = lax.ppermute(value, axis, forward)
    from_right = lax.ppermute(value, axis, backward)
    from_left2 = lax.ppermute(from_left, axis, forward)
    return jnp.stack([value, from_left, from_left2, from_right])


RING_SHIFT = (0, -1, -2, 1)


def local(hidden, queries, kv_panel, layout):
    block_len = hidden.shape[2]
    model_width = hidden.shape[3]
    heads_kv = kv_panel.shape[0]
    chunk_rows = kv_panel.shape[1]
    head_dim = kv_panel.shape[2] // 2
    group_size = queries.shape[3] // (heads_kv * head_dim)
    group_width = group_size * head_dim
    score_scale = head_dim ** (-0.5)
    n_chunks = model_width // chunk_rows
    x = lax.axis_index("x")
    y = lax.axis_index("y")
    zh = lax.axis_index("zh")
    core = lax.axis_index("core")
    fsdp = lax.axis_index("fsdp")
    ctx = ((x * 4 + y) * 2 + zh) * 2 + core
    block_table = layout[0]

    z_size = 2 * n_chunks
    forward = [(z, (z + 1) % z_size) for z in range(z_size)]
    backward = [(z, (z - 1) % z_size) for z in range(z_size)]
    mine = lax.dynamic_index_in_dim(kv_panel, core, 0, keepdims=False)
    panel = jnp.zeros((n_chunks,) + mine.shape, mine.dtype)
    panel = lax.dynamic_update_index_in_dim(panel, mine, fsdp, 0)
    going_up = mine
    going_down = mine
    for step in range(1, n_chunks // 2 + 1):
        going_up = lax.ppermute(going_up, ("zh", "fsdp"), forward)
        panel = lax.dynamic_update_index_in_dim(panel, going_up, (fsdp - step) % n_chunks, 0)
        if step < n_chunks // 2:
            going_down = lax.ppermute(going_down, ("zh", "fsdp"), backward)
            panel = lax.dynamic_update_index_in_dim(
                panel, going_down, (fsdp + step) % n_chunks, 0
            )
    panel = panel.reshape(model_width, 2 * head_dim)

    own_rows = hidden.reshape(2, block_len, model_width)
    token_rows = jnp.stack([own_rows, swap(own_rows, "core")])
    own_queries = queries.reshape(2, block_len, heads_kv, group_width)
    query_mine = lax.dynamic_index_in_dim(own_queries, core, 2, keepdims=False)
    query_other = lax.dynamic_index_in_dim(own_queries, 1 - core, 2, keepdims=False)
    query_blocks = jnp.stack([query_mine, swap(query_other, "core")])
    ctx_blocks = jnp.stack([ctx, ctx + 1 - 2 * core])
    own_blocks = block_table[ctx_blocks]

    projected = jnp.einsum(
        "bctd,de->bcte", token_rows, panel, preferred_element_type=jnp.float32
    )
    positions = own_blocks[:, None] * block_len + jnp.arange(block_len, dtype=jnp.int32)
    key_rows = rotate_keys(projected[..., :head_dim], positions[:, None, :], head_dim).astype(
        jnp.bfloat16
    )
    value_rows = projected[..., head_dim:].astype(jnp.bfloat16)

    clean = jnp.concatenate([key_rows[:, 0], value_rows[:, 0]], axis=-1)
    rows_all = 2 * block_len
    query_rows = query_blocks.reshape(2, rows_all, group_size, head_dim)
    row_limit = own_blocks[:, None] + jnp.concatenate(
        [jnp.ones((block_len,), jnp.int32), jnp.zeros((block_len,), jnp.int32)]
    )[None, :]
    shifts = jnp.array(RING_SHIFT, jnp.int32)
    pair = jnp.arange(2)

    def blocks_of(src_x, src_y, src_zh):
        src_core = (core + pair) % 2
        src = ((src_x[..., None] * 4 + src_y[..., None]) * 2 + src_zh) * 2 + src_core
        return block_table[src]

    def chain(rows, src_zh):
        fold_carry = empty_state(2, group_size, rows_all, head_dim)
        fold_carry = absorb_chunk(
            fold_carry, query_rows, rows, blocks_of(x, y, src_zh), row_limit, score_scale
        )
        along_x = ring4(rows, "x")
        src_x = (x + shifts) % 4
        for k in (1, 3, 2):
            fold_carry = absorb_chunk(
                fold_carry, query_rows, along_x[k], blocks_of(src_x[k], y, src_zh),
                row_limit, score_scale,
            )
        along_y = ring4(along_x, "y")
        src_y = (y + shifts) % 4
        for k in (1, 3, 2):
            fold_carry = absorb_chunk(
                fold_carry, query_rows, along_y[k],
                blocks_of(src_x, jnp.broadcast_to(src_y[k], (4,)), src_zh),
                row_limit, score_scale,
            )
        return fold_carry

    noisy_ok = jnp.broadcast_to((jnp.arange(rows_all) >= block_len)[:, None], (rows_all, block_len))
    noisy_state = jax.vmap(absorb, in_axes=(0, 0, 0, 0, None, None))(
        empty_state(2, group_size, rows_all, head_dim),
        query_rows, key_rows[:, 1], value_rows[:, 1], noisy_ok, score_scale,
    )
    near = chain(clean, zh)
    far = chain(swap(clean, "zh"), 1 - zh)
    highest, denominator, numerator = merge(merge(noisy_state, near), far)
    attended = jnp.transpose(numerator / denominator[..., None], (0, 2, 1, 3))
    attended = attended.astype(jnp.bfloat16).reshape(2, 2, block_len, group_width)
    returned = swap(attended[1], "core")
    first = jnp.where(core == 0, attended[0], returned)
    second = jnp.where(core == 0, returned, attended[0])
    result = jnp.concatenate([first, second], axis=-1)
    return result.reshape(2, 1, block_len, heads_kv * group_width)


def solution(mesh):
    axis_sizes = dict(zip(mesh.axis_names, mesh.devices.shape))
    assert axis_sizes["ctx"] == 64
    fine = Mesh(mesh.devices.reshape(4, 4, 2, 2, axis_sizes["fsdp"]), CTX + ("fsdp",))
    return jax.shard_map(
        local,
        mesh=fine,
        in_specs=(
            P(None, "fsdp", CTX, None),
            P(None, "fsdp", CTX, None),
            P(None, "fsdp", None),
            P("fsdp", None),
        ),
        out_specs=P(None, "fsdp", CTX, None),
        check_vma=False,
    )
```

```python
import math

import jax
import jax.numpy as jnp
from jax import lax
from jax.sharding import Mesh
from jax.sharding import PartitionSpec as P

NEGATIVE = -1e30
CTX = ("x", "y", "zh", "core")


def rotate_keys(vectors_in, positions, head_dim):
    half_dim = head_dim // 2
    inverse = 1000000.0 ** (-(jnp.arange(half_dim, dtype=jnp.float32) * 2.0 / head_dim))
    angles = positions.astype(jnp.float32)[..., None] * inverse
    cosine = jnp.cos(angles)
    sine_part = jnp.sin(angles)
    first_half = vectors_in[..., :half_dim]
    second_half = vectors_in[..., half_dim:]
    return jnp.concatenate(
        [
            first_half * cosine - second_half * sine_part,
            second_half * cosine + first_half * sine_part,
        ],
        axis=-1,
    )


def absorb(fold_carry, query_rows, key_part, value_part, allowed, score_scale):
    running, denominator, numerator = fold_carry
    scores = (
        jnp.einsum("tpd,ud->ptu", query_rows, key_part, preferred_element_type=jnp.float32)
        * score_scale
    )
    allowed_all = allowed[None]
    scores = jnp.where(allowed_all, scores, NEGATIVE)
    highest = jnp.maximum(running, jnp.max(scores, axis=-1))
    factor = jnp.exp(running - highest)
    weights = jnp.where(allowed_all, jnp.exp(scores - highest[..., None]), 0.0)
    denominator = denominator * factor + jnp.sum(weights, axis=-1)
    numerator = numerator * factor[..., None] + jnp.einsum(
        "ptu,ud->ptd",
        weights.astype(jnp.bfloat16),
        value_part,
        preferred_element_type=jnp.float32,
    )
    return (highest, denominator, numerator)


def absorb_tiled(fold_carry, query_rows, key_part, value_part, allowed, score_scale):
    key_count = key_part.shape[0]
    tile_width = math.gcd(key_count, 512)

    def one_tile(tile_index, inner):
        tile_start = tile_index * tile_width
        return absorb(
            inner,
            query_rows,
            lax.dynamic_slice_in_dim(key_part, tile_start, tile_width, 0),
            lax.dynamic_slice_in_dim(value_part, tile_start, tile_width, 0),
            lax.dynamic_slice_in_dim(allowed, tile_start, tile_width, 1),
            score_scale,
        )

    return lax.fori_loop(0, key_count // tile_width, one_tile, fold_carry)


def empty_state(blocks, group_size, rows_all, head_dim):
    return (
        jnp.full((blocks, group_size, rows_all), NEGATIVE, jnp.float32),
        jnp.zeros((blocks, group_size, rows_all), jnp.float32),
        jnp.zeros((blocks, group_size, rows_all, head_dim), jnp.float32),
    )


def absorb_chunk(fold_carry, query_rows, chunk, key_blocks, row_limit, score_scale):
    head_dim = query_rows.shape[-1]
    block_len = chunk.shape[-2]
    chunk = chunk.reshape(-1, 2 * head_dim)
    key_block = jnp.repeat(key_blocks.reshape(-1), block_len)
    allowed = key_block[None, None, :] < row_limit[:, :, None]
    return jax.vmap(absorb, in_axes=(0, 0, None, None, 0, None))(
        fold_carry, query_rows, chunk[:, :head_dim], chunk[:, head_dim:], allowed, score_scale
    )


def merge(first, second):
    high_a, den_a, num_a = first
    high_b, den_b, num_b = second
    highest = jnp.maximum(high_a, high_b)
    factor_a = jnp.exp(high_a - highest)
    factor_b = jnp.exp(high_b - highest)
    return (
        highest,
        den_a * factor_a + den_b * factor_b,
        num_a * factor_a[..., None] + num_b * factor_b[..., None],
    )


def swap(value, axis):
    return lax.ppermute(value, axis, [(0, 1), (1, 0)])


def ring4(value, axis):
    size = 4
    forward = [(i, (i + 1) % size) for i in range(size)]
    backward = [(i, (i - 1) % size) for i in range(size)]
    from_left = lax.ppermute(value, axis, forward)
    from_right = lax.ppermute(value, axis, backward)
    from_left2 = lax.ppermute(from_left, axis, forward)
    return jnp.stack([value, from_left, from_left2, from_right])


RING_SHIFT = (0, -1, -2, 1)


def local(hidden, queries, kv_panel, layout):
    block_len = hidden.shape[2]
    model_width = hidden.shape[3]
    heads_kv = kv_panel.shape[0]
    chunk_rows = kv_panel.shape[1]
    head_dim = kv_panel.shape[2] // 2
    group_size = queries.shape[3] // (heads_kv * head_dim)
    group_width = group_size * head_dim
    score_scale = head_dim ** (-0.5)
    n_chunks = model_width // chunk_rows
    x = lax.axis_index("x")
    y = lax.axis_index("y")
    zh = lax.axis_index("zh")
    core = lax.axis_index("core")
    fsdp = lax.axis_index("fsdp")
    ctx = ((x * 4 + y) * 2 + zh) * 2 + core
    block_table = layout[0]

    z_size = 2 * n_chunks
    forward = [(z, (z + 1) % z_size) for z in range(z_size)]
    backward = [(z, (z - 1) % z_size) for z in range(z_size)]
    mine = lax.dynamic_index_in_dim(kv_panel, core, 0, keepdims=False)
    panel = jnp.zeros((n_chunks,) + mine.shape, mine.dtype)
    panel = lax.dynamic_update_index_in_dim(panel, mine, fsdp, 0)
    going_up = mine
    going_down = mine
    for step in range(1, n_chunks // 2 + 1):
        going_up = lax.ppermute(going_up, ("zh", "fsdp"), forward)
        panel = lax.dynamic_update_index_in_dim(panel, going_up, (fsdp - step) % n_chunks, 0)
        if step < n_chunks // 2:
            going_down = lax.ppermute(going_down, ("zh", "fsdp"), backward)
            panel = lax.dynamic_update_index_in_dim(
                panel, going_down, (fsdp + step) % n_chunks, 0
            )
    panel = panel.reshape(model_width, 2 * head_dim)

    own_rows = hidden.reshape(2, block_len, model_width)
    token_rows = jnp.stack([own_rows, swap(own_rows, "core")])
    own_queries = queries.reshape(2, block_len, heads_kv, group_width)
    query_mine = lax.dynamic_index_in_dim(own_queries, core, 2, keepdims=False)
    query_other = lax.dynamic_index_in_dim(own_queries, 1 - core, 2, keepdims=False)
    query_blocks = jnp.stack([query_mine, swap(query_other, "core")])
    ctx_blocks = jnp.stack([ctx, ctx + 1 - 2 * core])
    own_blocks = block_table[ctx_blocks]

    projected = jnp.einsum(
        "bctd,de->bcte", token_rows, panel, preferred_element_type=jnp.float32
    )
    positions = own_blocks[:, None] * block_len + jnp.arange(block_len, dtype=jnp.int32)
    key_rows = rotate_keys(projected[..., :head_dim], positions[:, None, :], head_dim).astype(
        jnp.bfloat16
    )
    value_rows = projected[..., head_dim:].astype(jnp.bfloat16)

    clean = jnp.concatenate([key_rows[:, 0], value_rows[:, 0]], axis=-1)
    rows_all = 2 * block_len
    query_rows = query_blocks.reshape(2, rows_all, group_size, head_dim)
    row_limit = own_blocks[:, None] + jnp.concatenate(
        [jnp.ones((block_len,), jnp.int32), jnp.zeros((block_len,), jnp.int32)]
    )[None, :]
    shifts = jnp.array(RING_SHIFT, jnp.int32)
    src_x = (x + shifts) % 4
    src_y = (y + shifts) % 4
    src_zh = (zh + jnp.arange(2)) % 2
    src_core = (core + jnp.arange(2)) % 2
    src = (
        (src_x[None, None, :, None] * 4 + src_y[None, :, None, None]) * 2
        + src_zh[:, None, None, None]
    ) * 2 + src_core
    every_block = block_table[src.reshape(-1)].reshape(2, 4, 4, 2)

    def chain(rows, side):
        blocks = every_block[side]
        fold_carry = empty_state(2, group_size, rows_all, head_dim)
        fold_carry = absorb_chunk(
            fold_carry, query_rows, rows, blocks[0, 0], row_limit, score_scale
        )
        along_x = ring4(rows, "x")
        fold_carry = absorb_chunk(
            fold_carry, query_rows, along_x[1::2], blocks[0, 1::2], row_limit, score_scale
        )
        fold_carry = absorb_chunk(
            fold_carry, query_rows, along_x[2], blocks[0, 2], row_limit, score_scale
        )
        along_y = ring4(along_x, "y")
        fold_carry = absorb_chunk(
            fold_carry, query_rows, along_y[1::2], blocks[1::2], row_limit, score_scale
        )
        fold_carry = absorb_chunk(
            fold_carry, query_rows, along_y[2], blocks[2], row_limit, score_scale
        )
        return fold_carry

    noisy_ok = jnp.broadcast_to((jnp.arange(rows_all) >= block_len)[:, None], (rows_all, block_len))
    noisy_state = jax.vmap(absorb, in_axes=(0, 0, 0, 0, None, None))(
        empty_state(2, group_size, rows_all, head_dim),
        query_rows, key_rows[:, 1], value_rows[:, 1], noisy_ok, score_scale,
    )
    near = chain(clean, 0)
    far = chain(swap(clean, "zh"), 1)
    highest, denominator, numerator = merge(merge(noisy_state, near), far)
    attended = jnp.transpose(numerator / denominator[..., None], (0, 2, 1, 3))
    attended = attended.astype(jnp.bfloat16).reshape(2, 2, block_len, group_width)
    returned = swap(attended[1], "core")
    first = jnp.where(core == 0, attended[0], returned)
    second = jnp.where(core == 0, returned, attended[0])
    result = jnp.concatenate([first, second], axis=-1)
    return result.reshape(2, 1, block_len, heads_kv * group_width)


def solution(mesh):
    axis_sizes = dict(zip(mesh.axis_names, mesh.devices.shape))
    assert axis_sizes["ctx"] == 64
    fine = Mesh(mesh.devices.reshape(4, 4, 2, 2, axis_sizes["fsdp"]), CTX + ("fsdp",))
    return jax.shard_map(
        local,
        mesh=fine,
        in_specs=(
            P(None, "fsdp", CTX, None),
            P(None, "fsdp", CTX, None),
            P(None, "fsdp", None),
            P("fsdp", None),
        ),
        out_specs=P(None, "fsdp", CTX, None),
        check_vma=False,
    )
```

```python
import math

import jax
import jax.numpy as jnp
from jax import lax
from jax.sharding import Mesh
from jax.sharding import PartitionSpec as P

NEGATIVE = -1e30
CTX = ("x", "y", "zh", "core")


def rotate_keys(vectors_in, positions, head_dim):
    half_dim = head_dim // 2
    inverse = 1000000.0 ** (-(jnp.arange(half_dim, dtype=jnp.float32) * 2.0 / head_dim))
    angles = positions.astype(jnp.float32)[..., None] * inverse
    cosine = jnp.cos(angles)
    sine_part = jnp.sin(angles)
    first_half = vectors_in[..., :half_dim]
    second_half = vectors_in[..., half_dim:]
    return jnp.concatenate(
        [
            first_half * cosine - second_half * sine_part,
            second_half * cosine + first_half * sine_part,
        ],
        axis=-1,
    )


def absorb(fold_carry, query_rows, key_part, value_part, allowed, score_scale):
    running, denominator, numerator = fold_carry
    scores = (
        jnp.einsum("tpd,ud->ptu", query_rows, key_part, preferred_element_type=jnp.float32)
        * score_scale
    )
    allowed_all = allowed[None]
    scores = jnp.where(allowed_all, scores, NEGATIVE)
    highest = jnp.maximum(running, jnp.max(scores, axis=-1))
    factor = jnp.exp(running - highest)
    weights = jnp.where(allowed_all, jnp.exp(scores - highest[..., None]), 0.0)
    denominator = denominator * factor + jnp.sum(weights, axis=-1)
    numerator = numerator * factor[..., None] + jnp.einsum(
        "ptu,ud->ptd",
        weights.astype(jnp.bfloat16),
        value_part,
        preferred_element_type=jnp.float32,
    )
    return (highest, denominator, numerator)


def absorb_tiled(fold_carry, query_rows, key_part, value_part, allowed, score_scale):
    key_count = key_part.shape[0]
    tile_width = math.gcd(key_count, 512)

    def one_tile(tile_index, inner):
        tile_start = tile_index * tile_width
        return absorb(
            inner,
            query_rows,
            lax.dynamic_slice_in_dim(key_part, tile_start, tile_width, 0),
            lax.dynamic_slice_in_dim(value_part, tile_start, tile_width, 0),
            lax.dynamic_slice_in_dim(allowed, tile_start, tile_width, 1),
            score_scale,
        )

    return lax.fori_loop(0, key_count // tile_width, one_tile, fold_carry)


def empty_state(blocks, group_size, rows_all, head_dim):
    return (
        jnp.full((blocks, group_size, rows_all), NEGATIVE, jnp.float32),
        jnp.zeros((blocks, group_size, rows_all), jnp.float32),
        jnp.zeros((blocks, group_size, rows_all, head_dim), jnp.float32),
    )


def absorb_chunk(fold_carry, query_rows, chunk, key_blocks, row_limit, score_scale):
    head_dim = query_rows.shape[-1]
    block_len = chunk.shape[-2]
    chunk = chunk.reshape(-1, 2 * head_dim)
    key_block = jnp.repeat(key_blocks.reshape(-1), block_len)
    allowed = key_block[None, None, :] < row_limit[:, :, None]
    return jax.vmap(absorb, in_axes=(0, 0, None, None, 0, None))(
        fold_carry, query_rows, chunk[:, :head_dim], chunk[:, head_dim:], allowed, score_scale
    )


def merge(first, second):
    high_a, den_a, num_a = first
    high_b, den_b, num_b = second
    highest = jnp.maximum(high_a, high_b)
    factor_a = jnp.exp(high_a - highest)
    factor_b = jnp.exp(high_b - highest)
    return (
        highest,
        den_a * factor_a + den_b * factor_b,
        num_a * factor_a[..., None] + num_b * factor_b[..., None],
    )


def swap(value, axis):
    return lax.ppermute(value, axis, [(0, 1), (1, 0)])


def local(hidden, queries, kv_panel, layout):
    block_len = hidden.shape[2]
    model_width = hidden.shape[3]
    heads_kv = kv_panel.shape[0]
    chunk_rows = kv_panel.shape[1]
    head_dim = kv_panel.shape[2] // 2
    group_size = queries.shape[3] // (heads_kv * head_dim)
    group_width = group_size * head_dim
    score_scale = head_dim ** (-0.5)
    n_chunks = model_width // chunk_rows
    x = lax.axis_index("x")
    y = lax.axis_index("y")
    zh = lax.axis_index("zh")
    core = lax.axis_index("core")
    fsdp = lax.axis_index("fsdp")
    ctx = ((x * 4 + y) * 2 + zh) * 2 + core
    block_table = layout[0]

    z_size = 2 * n_chunks
    forward = [(z, (z + 1) % z_size) for z in range(z_size)]
    backward = [(z, (z - 1) % z_size) for z in range(z_size)]
    mine = lax.dynamic_index_in_dim(kv_panel, core, 0, keepdims=False)
    panel = jnp.zeros((n_chunks,) + mine.shape, mine.dtype)
    panel = lax.dynamic_update_index_in_dim(panel, mine, fsdp, 0)
    going_up = mine
    going_down = mine
    for step in range(1, n_chunks // 2 + 1):
        going_up = lax.ppermute(going_up, ("zh", "fsdp"), forward)
        panel = lax.dynamic_update_index_in_dim(panel, going_up, (fsdp - step) % n_chunks, 0)
        if step < n_chunks // 2:
            going_down = lax.ppermute(going_down, ("zh", "fsdp"), backward)
            panel = lax.dynamic_update_index_in_dim(
                panel, going_down, (fsdp + step) % n_chunks, 0
            )
    panel = panel.reshape(model_width, 2 * head_dim)

    own_rows = hidden.reshape(2, block_len, model_width)
    token_rows = jnp.stack([own_rows, swap(own_rows, "core")])
    own_queries = queries.reshape(2, block_len, heads_kv, group_width)
    query_mine = lax.dynamic_index_in_dim(own_queries, core, 2, keepdims=False)
    query_other = lax.dynamic_index_in_dim(own_queries, 1 - core, 2, keepdims=False)
    query_blocks = jnp.stack([query_mine, swap(query_other, "core")])
    ctx_blocks = jnp.stack([ctx, ctx + 1 - 2 * core])
    own_blocks = block_table[ctx_blocks]

    projected = jnp.einsum(
        "bctd,de->bcte", token_rows, panel, preferred_element_type=jnp.float32
    )
    positions = own_blocks[:, None] * block_len + jnp.arange(block_len, dtype=jnp.int32)
    key_rows = rotate_keys(projected[..., :head_dim], positions[:, None, :], head_dim).astype(
        jnp.bfloat16
    )
    value_rows = projected[..., head_dim:].astype(jnp.bfloat16)

    clean = jnp.concatenate([key_rows[:, 0], value_rows[:, 0]], axis=-1)
    rows_all = 2 * block_len
    query_rows = query_blocks.reshape(2, rows_all, group_size, head_dim)
    row_limit = own_blocks[:, None] + jnp.concatenate(
        [jnp.ones((block_len,), jnp.int32), jnp.zeros((block_len,), jnp.int32)]
    )[None, :]
    src_x = jnp.arange(4)
    src_y = jnp.arange(4)
    src_zh = (zh + jnp.arange(2)) % 2
    src_core = (core + jnp.arange(2)) % 2
    src = (
        (src_x[None, None, :, None] * 4 + src_y[None, :, None, None]) * 2
        + src_zh[:, None, None, None]
    ) * 2 + src_core
    every_block = block_table[src.reshape(-1)].reshape(2, 4, 4, 2)

    def chain(rows, side):
        blocks = jnp.swapaxes(every_block[side], 0, 1).reshape(-1, 4, 2)
        spread = jnp.broadcast_to(rows[None], (16,) + rows.shape)
        gathered = lax.all_to_all(spread, ("x", "y"), 0, 0, tiled=True).reshape(-1, 4, *rows.shape)
        fold_carry = empty_state(2, group_size, rows_all, head_dim)
        for part in range(gathered.shape[0]):
            fold_carry = absorb_chunk(
                fold_carry, query_rows, gathered[part], blocks[part], row_limit, score_scale
            )
        return fold_carry

    noisy_ok = jnp.broadcast_to((jnp.arange(rows_all) >= block_len)[:, None], (rows_all, block_len))
    noisy_state = jax.vmap(absorb, in_axes=(0, 0, 0, 0, None, None))(
        empty_state(2, group_size, rows_all, head_dim),
        query_rows, key_rows[:, 1], value_rows[:, 1], noisy_ok, score_scale,
    )
    near = chain(clean, 0)
    far = chain(swap(clean, "zh"), 1)
    highest, denominator, numerator = merge(merge(noisy_state, near), far)
    attended = jnp.transpose(numerator / denominator[..., None], (0, 2, 1, 3))
    attended = attended.astype(jnp.bfloat16).reshape(2, 2, block_len, group_width)
    returned = swap(attended[1], "core")
    first = jnp.where(core == 0, attended[0], returned)
    second = jnp.where(core == 0, returned, attended[0])
    result = jnp.concatenate([first, second], axis=-1)
    return result.reshape(2, 1, block_len, heads_kv * group_width)


def solution(mesh):
    axis_sizes = dict(zip(mesh.axis_names, mesh.devices.shape))
    assert axis_sizes["ctx"] == 64
    fine = Mesh(mesh.devices.reshape(4, 4, 2, 2, axis_sizes["fsdp"]), CTX + ("fsdp",))
    return jax.shard_map(
        local,
        mesh=fine,
        in_specs=(
            P(None, "fsdp", CTX, None),
            P(None, "fsdp", CTX, None),
            P(None, "fsdp", None),
            P("fsdp", None),
        ),
        out_specs=P(None, "fsdp", CTX, None),
        check_vma=False,
    )
```

```python
import math

import jax
import jax.numpy as jnp
from jax import lax
from jax.sharding import Mesh
from jax.sharding import PartitionSpec as P

NEGATIVE = -1e30
CTX = ("x", "y", "zh", "core")


def rotate_keys(vectors_in, positions, head_dim):
    half_dim = head_dim // 2
    inverse = 1000000.0 ** (-(jnp.arange(half_dim, dtype=jnp.float32) * 2.0 / head_dim))
    angles = positions.astype(jnp.float32)[..., None] * inverse
    cosine = jnp.cos(angles)
    sine_part = jnp.sin(angles)
    first_half = vectors_in[..., :half_dim]
    second_half = vectors_in[..., half_dim:]
    return jnp.concatenate(
        [
            first_half * cosine - second_half * sine_part,
            second_half * cosine + first_half * sine_part,
        ],
        axis=-1,
    )


def absorb(fold_carry, query_rows, key_part, value_part, allowed, score_scale):
    running, denominator, numerator = fold_carry
    scores = (
        jnp.einsum("tpd,ud->ptu", query_rows, key_part, preferred_element_type=jnp.float32)
        * score_scale
    )
    allowed_all = allowed[None]
    scores = jnp.where(allowed_all, scores, NEGATIVE)
    highest = jnp.maximum(running, jnp.max(scores, axis=-1))
    factor = jnp.exp(running - highest)
    weights = jnp.where(allowed_all, jnp.exp(scores - highest[..., None]), 0.0)
    denominator = denominator * factor + jnp.sum(weights, axis=-1)
    numerator = numerator * factor[..., None] + jnp.einsum(
        "ptu,ud->ptd",
        weights.astype(jnp.bfloat16),
        value_part,
        preferred_element_type=jnp.float32,
    )
    return (highest, denominator, numerator)


def absorb_tiled(fold_carry, query_rows, key_part, value_part, allowed, score_scale):
    key_count = key_part.shape[0]
    tile_width = math.gcd(key_count, 512)

    def one_tile(tile_index, inner):
        tile_start = tile_index * tile_width
        return absorb(
            inner,
            query_rows,
            lax.dynamic_slice_in_dim(key_part, tile_start, tile_width, 0),
            lax.dynamic_slice_in_dim(value_part, tile_start, tile_width, 0),
            lax.dynamic_slice_in_dim(allowed, tile_start, tile_width, 1),
            score_scale,
        )

    return lax.fori_loop(0, key_count // tile_width, one_tile, fold_carry)


def empty_state(blocks, group_size, rows_all, head_dim):
    return (
        jnp.full((blocks, group_size, rows_all), NEGATIVE, jnp.float32),
        jnp.zeros((blocks, group_size, rows_all), jnp.float32),
        jnp.zeros((blocks, group_size, rows_all, head_dim), jnp.float32),
    )


def absorb_chunk(fold_carry, query_rows, chunk, key_blocks, row_limit, score_scale):
    head_dim = query_rows.shape[-1]
    block_len = chunk.shape[-2]
    chunk = chunk.reshape(-1, 2 * head_dim)
    key_block = jnp.repeat(key_blocks.reshape(-1), block_len)
    allowed = key_block[None, None, :] < row_limit[:, :, None]
    return jax.vmap(absorb, in_axes=(0, 0, None, None, 0, None))(
        fold_carry, query_rows, chunk[:, :head_dim], chunk[:, head_dim:], allowed, score_scale
    )


def merge(first, second):
    high_a, den_a, num_a = first
    high_b, den_b, num_b = second
    highest = jnp.maximum(high_a, high_b)
    factor_a = jnp.exp(high_a - highest)
    factor_b = jnp.exp(high_b - highest)
    return (
        highest,
        den_a * factor_a + den_b * factor_b,
        num_a * factor_a[..., None] + num_b * factor_b[..., None],
    )


def swap(value, axis):
    return lax.ppermute(value, axis, [(0, 1), (1, 0)])


def local(hidden, queries, kv_panel, layout):
    block_len = hidden.shape[2]
    model_width = hidden.shape[3]
    heads_kv = kv_panel.shape[0]
    chunk_rows = kv_panel.shape[1]
    head_dim = kv_panel.shape[2] // 2
    group_size = queries.shape[3] // (heads_kv * head_dim)
    group_width = group_size * head_dim
    score_scale = head_dim ** (-0.5)
    n_chunks = model_width // chunk_rows
    x = lax.axis_index("x")
    y = lax.axis_index("y")
    zh = lax.axis_index("zh")
    core = lax.axis_index("core")
    fsdp = lax.axis_index("fsdp")
    ctx = ((x * 4 + y) * 2 + zh) * 2 + core
    block_table = layout[0]

    z_size = 2 * n_chunks
    forward = [(z, (z + 1) % z_size) for z in range(z_size)]
    backward = [(z, (z - 1) % z_size) for z in range(z_size)]
    mine = lax.dynamic_index_in_dim(kv_panel, core, 0, keepdims=False)
    going_up = mine
    going_down = mine
    from_below = []
    from_above = []
    for step in range(1, n_chunks // 2 + 1):
        going_up = lax.ppermute(going_up, ("zh", "fsdp"), forward)
        from_below.append(going_up)
        if step < n_chunks // 2:
            going_down = lax.ppermute(going_down, ("zh", "fsdp"), backward)
            from_above.append(going_down)
    panel = jnp.concatenate([mine] + from_above + from_below[::-1], axis=0)

    own_rows = hidden.reshape(2, block_len, model_width)
    token_rows = jnp.stack([own_rows, swap(own_rows, "core")])
    token_rows = jnp.roll(token_rows, -fsdp * chunk_rows, axis=-1)
    own_queries = queries.reshape(2, block_len, heads_kv, group_width)
    query_mine = lax.dynamic_index_in_dim(own_queries, core, 2, keepdims=False)
    query_other = lax.dynamic_index_in_dim(own_queries, 1 - core, 2, keepdims=False)
    query_blocks = jnp.stack([query_mine, swap(query_other, "core")])
    ctx_blocks = jnp.stack([ctx, ctx + 1 - 2 * core])
    own_blocks = block_table[ctx_blocks]

    projected = jnp.einsum(
        "bctd,de->bcte", token_rows, panel, preferred_element_type=jnp.float32
    )
    positions = own_blocks[:, None] * block_len + jnp.arange(block_len, dtype=jnp.int32)
    key_rows = rotate_keys(projected[..., :head_dim], positions[:, None, :], head_dim).astype(
        jnp.bfloat16
    )
    value_rows = projected[..., head_dim:].astype(jnp.bfloat16)

    clean = jnp.concatenate([key_rows[:, 0], value_rows[:, 0]], axis=-1)
    rows_all = 2 * block_len
    query_rows = query_blocks.reshape(2, rows_all, group_size, head_dim)
    row_limit = own_blocks[:, None] + jnp.concatenate(
        [jnp.ones((block_len,), jnp.int32), jnp.zeros((block_len,), jnp.int32)]
    )[None, :]
    src_x = jnp.arange(4)
    src_y = jnp.arange(4)
    src_zh = (zh + jnp.arange(2)) % 2
    src_core = (core + jnp.arange(2)) % 2
    src = (
        (src_x[None, None, :, None] * 4 + src_y[None, :, None, None]) * 2
        + src_zh[:, None, None, None]
    ) * 2 + src_core
    every_block = block_table[src.reshape(-1)].reshape(2, 4, 4, 2)

    def chain(rows, side):
        blocks = jnp.swapaxes(every_block[side], 0, 1).reshape(-1, 4, 2)
        spread = jnp.broadcast_to(rows[None], (16,) + rows.shape)
        gathered = lax.all_to_all(spread, ("x", "y"), 0, 0, tiled=True).reshape(-1, 4, *rows.shape)
        fold_carry = empty_state(2, group_size, rows_all, head_dim)
        for part in range(gathered.shape[0]):
            fold_carry = absorb_chunk(
                fold_carry, query_rows, gathered[part], blocks[part], row_limit, score_scale
            )
        return fold_carry

    noisy_ok = jnp.broadcast_to((jnp.arange(rows_all) >= block_len)[:, None], (rows_all, block_len))
    noisy_state = jax.vmap(absorb, in_axes=(0, 0, 0, 0, None, None))(
        empty_state(2, group_size, rows_all, head_dim),
        query_rows, key_rows[:, 1], value_rows[:, 1], noisy_ok, score_scale,
    )
    near = chain(clean, 0)
    far = chain(swap(clean, "zh"), 1)
    highest, denominator, numerator = merge(merge(noisy_state, near), far)
    attended = jnp.transpose(numerator / denominator[..., None], (0, 2, 1, 3))
    attended = attended.astype(jnp.bfloat16).reshape(2, 2, block_len, group_width)
    returned = swap(attended[1], "core")
    first = jnp.where(core == 0, attended[0], returned)
    second = jnp.where(core == 0, returned, attended[0])
    result = jnp.concatenate([first, second], axis=-1)
    return result.reshape(2, 1, block_len, heads_kv * group_width)


def solution(mesh):
    axis_sizes = dict(zip(mesh.axis_names, mesh.devices.shape))
    assert axis_sizes["ctx"] == 64
    fine = Mesh(mesh.devices.reshape(4, 4, 2, 2, axis_sizes["fsdp"]), CTX + ("fsdp",))
    return jax.shard_map(
        local,
        mesh=fine,
        in_specs=(
            P(None, "fsdp", CTX, None),
            P(None, "fsdp", CTX, None),
            P(None, "fsdp", None),
            P("fsdp", None),
        ),
        out_specs=P(None, "fsdp", CTX, None),
        check_vma=False,
    )
```

```python
import math

import jax
import jax.numpy as jnp
from jax import lax
from jax.sharding import Mesh
from jax.sharding import PartitionSpec as P

NEGATIVE = -1e30
CTX = ("x", "y", "zh", "core")


def rotate_keys(vectors_in, positions, head_dim):
    half_dim = head_dim // 2
    inverse = 1000000.0 ** (-(jnp.arange(half_dim, dtype=jnp.float32) * 2.0 / head_dim))
    angles = positions.astype(jnp.float32)[..., None] * inverse
    cosine = jnp.cos(angles)
    sine_part = jnp.sin(angles)
    first_half = vectors_in[..., :half_dim]
    second_half = vectors_in[..., half_dim:]
    return jnp.concatenate(
        [
            first_half * cosine - second_half * sine_part,
            second_half * cosine + first_half * sine_part,
        ],
        axis=-1,
    )


def absorb(fold_carry, query_rows, key_part, value_part, allowed, score_scale):
    running, denominator, numerator = fold_carry
    scores = (
        jnp.einsum("tpd,ud->ptu", query_rows, key_part, preferred_element_type=jnp.float32)
        * score_scale
    )
    allowed_all = allowed[None]
    scores = jnp.where(allowed_all, scores, NEGATIVE)
    highest = jnp.maximum(running, jnp.max(scores, axis=-1))
    factor = jnp.exp(running - highest)
    weights = jnp.where(allowed_all, jnp.exp(scores - highest[..., None]), 0.0)
    denominator = denominator * factor + jnp.sum(weights, axis=-1)
    numerator = numerator * factor[..., None] + jnp.einsum(
        "ptu,ud->ptd",
        weights.astype(jnp.bfloat16),
        value_part,
        preferred_element_type=jnp.float32,
    )
    return (highest, denominator, numerator)


def absorb_tiled(fold_carry, query_rows, key_part, value_part, allowed, score_scale):
    key_count = key_part.shape[0]
    tile_width = math.gcd(key_count, 512)

    def one_tile(tile_index, inner):
        tile_start = tile_index * tile_width
        return absorb(
            inner,
            query_rows,
            lax.dynamic_slice_in_dim(key_part, tile_start, tile_width, 0),
            lax.dynamic_slice_in_dim(value_part, tile_start, tile_width, 0),
            lax.dynamic_slice_in_dim(allowed, tile_start, tile_width, 1),
            score_scale,
        )

    return lax.fori_loop(0, key_count // tile_width, one_tile, fold_carry)


def empty_state(blocks, group_size, rows_all, head_dim):
    return (
        jnp.full((blocks, group_size, rows_all), NEGATIVE, jnp.float32),
        jnp.zeros((blocks, group_size, rows_all), jnp.float32),
        jnp.zeros((blocks, group_size, rows_all, head_dim), jnp.float32),
    )


def absorb_chunk(fold_carry, query_rows, chunk, key_blocks, row_limit, score_scale):
    head_dim = query_rows.shape[-1]
    block_len = chunk.shape[-2]
    chunk = chunk.reshape(-1, 2 * head_dim)
    key_block = jnp.repeat(key_blocks.reshape(-1), block_len)
    allowed = key_block[None, None, :] < row_limit[:, :, None]
    return jax.vmap(absorb, in_axes=(0, 0, None, None, 0, None))(
        fold_carry, query_rows, chunk[:, :head_dim], chunk[:, head_dim:], allowed, score_scale
    )


def merge(first, second):
    high_a, den_a, num_a = first
    high_b, den_b, num_b = second
    highest = jnp.maximum(high_a, high_b)
    factor_a = jnp.exp(high_a - highest)
    factor_b = jnp.exp(high_b - highest)
    return (
        highest,
        den_a * factor_a + den_b * factor_b,
        num_a * factor_a[..., None] + num_b * factor_b[..., None],
    )


def swap(value, axis):
    return lax.ppermute(value, axis, [(0, 1), (1, 0)])


def local(hidden, queries, kv_panel, layout):
    block_len = hidden.shape[2]
    model_width = hidden.shape[3]
    heads_kv = kv_panel.shape[0]
    chunk_rows = kv_panel.shape[1]
    head_dim = kv_panel.shape[2] // 2
    group_size = queries.shape[3] // (heads_kv * head_dim)
    group_width = group_size * head_dim
    score_scale = head_dim ** (-0.5)
    n_chunks = model_width // chunk_rows
    x = lax.axis_index("x")
    y = lax.axis_index("y")
    zh = lax.axis_index("zh")
    core = lax.axis_index("core")
    fsdp = lax.axis_index("fsdp")
    ctx = ((x * 4 + y) * 2 + zh) * 2 + core
    block_table = layout[0]

    z_size = 2 * n_chunks
    forward = [(z, (z + 1) % z_size) for z in range(z_size)]
    backward = [(z, (z - 1) % z_size) for z in range(z_size)]
    mine = lax.dynamic_index_in_dim(kv_panel, core, 0, keepdims=False)
    going_up = mine
    going_down = mine
    from_below = []
    from_above = []
    for step in range(1, n_chunks // 2 + 1):
        going_up = lax.ppermute(going_up, ("zh", "fsdp"), forward)
        from_below.append(going_up)
        if step < n_chunks // 2:
            going_down = lax.ppermute(going_down, ("zh", "fsdp"), backward)
            from_above.append(going_down)
    panel = jnp.concatenate([mine] + from_above + from_below[::-1], axis=0)

    own_rows = hidden.reshape(2, block_len, model_width)
    token_rows = jnp.stack([own_rows, swap(own_rows, "core")])
    token_rows = jnp.roll(token_rows, -fsdp * chunk_rows, axis=-1)
    own_queries = queries.reshape(2, block_len, heads_kv, group_width)
    query_mine = lax.dynamic_index_in_dim(own_queries, core, 2, keepdims=False)
    query_other = lax.dynamic_index_in_dim(own_queries, 1 - core, 2, keepdims=False)
    query_blocks = jnp.stack([query_mine, swap(query_other, "core")])
    ctx_blocks = jnp.stack([ctx, ctx + 1 - 2 * core])
    own_blocks = block_table[ctx_blocks]

    projected = jnp.einsum(
        "bctd,de->bcte", token_rows, panel, preferred_element_type=jnp.float32
    )
    positions = own_blocks[:, None] * block_len + jnp.arange(block_len, dtype=jnp.int32)
    key_rows = rotate_keys(projected[..., :head_dim], positions[:, None, :], head_dim).astype(
        jnp.bfloat16
    )
    value_rows = projected[..., head_dim:].astype(jnp.bfloat16)

    clean = jnp.concatenate([key_rows[:, 0], value_rows[:, 0]], axis=-1)
    rows_all = 2 * block_len
    query_rows = query_blocks.reshape(2, rows_all, group_size, head_dim)
    row_limit = own_blocks[:, None] + jnp.concatenate(
        [jnp.ones((block_len,), jnp.int32), jnp.zeros((block_len,), jnp.int32)]
    )[None, :]
    src_x = jnp.arange(4)
    src_y = jnp.arange(4)
    src_zh = (zh + jnp.arange(2)) % 2
    src_core = (core + jnp.arange(2)) % 2
    src = (
        (src_x[None, None, :, None] * 4 + src_y[None, :, None, None]) * 2
        + src_zh[:, None, None, None]
    ) * 2 + src_core
    every_block = block_table[src.reshape(-1)].reshape(2, 4, 4, 2)

    visible = jnp.max(own_blocks) + 1

    def chain(rows, side):
        blocks = jnp.swapaxes(every_block[side], 0, 1).reshape(-1)
        spread = jnp.broadcast_to(rows[None], (16,) + rows.shape)
        gathered = lax.all_to_all(spread, ("x", "y"), 0, 0, tiled=True)
        gathered = gathered.reshape(blocks.shape[0], block_len, 2 * head_dim)
        rank = jnp.sum(blocks[None, :] < blocks[:, None], axis=1)
        order = jnp.argmax(rank[None, :] == jnp.arange(blocks.shape[0])[:, None], axis=1)
        sorted_rows = gathered[order]
        sorted_blocks = blocks[order]
        tile_blocks = 8
        tiles = (jnp.sum(blocks < visible) + tile_blocks - 1) // tile_blocks

        def one_tile(tile_index, fold_carry):
            first = tile_index * tile_blocks
            return absorb_chunk(
                fold_carry, query_rows,
                lax.dynamic_slice_in_dim(sorted_rows, first, tile_blocks, 0),
                lax.dynamic_slice_in_dim(sorted_blocks, first, tile_blocks, 0),
                row_limit, score_scale,
            )

        fold_carry = empty_state(2, group_size, rows_all, head_dim)
        return lax.fori_loop(0, tiles, one_tile, fold_carry)

    noisy_ok = jnp.broadcast_to((jnp.arange(rows_all) >= block_len)[:, None], (rows_all, block_len))
    noisy_state = jax.vmap(absorb, in_axes=(0, 0, 0, 0, None, None))(
        empty_state(2, group_size, rows_all, head_dim),
        query_rows, key_rows[:, 1], value_rows[:, 1], noisy_ok, score_scale,
    )
    near = chain(clean, 0)
    far = chain(swap(clean, "zh"), 1)
    highest, denominator, numerator = merge(merge(noisy_state, near), far)
    attended = jnp.transpose(numerator / denominator[..., None], (0, 2, 1, 3))
    attended = attended.astype(jnp.bfloat16).reshape(2, 2, block_len, group_width)
    returned = swap(attended[1], "core")
    first = jnp.where(core == 0, attended[0], returned)
    second = jnp.where(core == 0, returned, attended[0])
    result = jnp.concatenate([first, second], axis=-1)
    return result.reshape(2, 1, block_len, heads_kv * group_width)


def solution(mesh):
    axis_sizes = dict(zip(mesh.axis_names, mesh.devices.shape))
    assert axis_sizes["ctx"] == 64
    fine = Mesh(mesh.devices.reshape(4, 4, 2, 2, axis_sizes["fsdp"]), CTX + ("fsdp",))
    return jax.shard_map(
        local,
        mesh=fine,
        in_specs=(
            P(None, "fsdp", CTX, None),
            P(None, "fsdp", CTX, None),
            P(None, "fsdp", None),
            P("fsdp", None),
        ),
        out_specs=P(None, "fsdp", CTX, None),
        check_vma=False,
    )
```

```python
import math

import jax
import jax.numpy as jnp
from jax import lax
from jax.sharding import Mesh
from jax.sharding import PartitionSpec as P

NEGATIVE = -1e30
CTX = ("x", "y", "zh", "core")


def rotate_keys(vectors_in, positions, head_dim):
    half_dim = head_dim // 2
    inverse = 1000000.0 ** (-(jnp.arange(half_dim, dtype=jnp.float32) * 2.0 / head_dim))
    angles = positions.astype(jnp.float32)[..., None] * inverse
    cosine = jnp.cos(angles)
    sine_part = jnp.sin(angles)
    first_half = vectors_in[..., :half_dim]
    second_half = vectors_in[..., half_dim:]
    return jnp.concatenate(
        [
            first_half * cosine - second_half * sine_part,
            second_half * cosine + first_half * sine_part,
        ],
        axis=-1,
    )


def absorb(fold_carry, query_rows, key_part, value_part, allowed, score_scale):
    running, denominator, numerator = fold_carry
    scores = (
        jnp.einsum("tpd,ud->ptu", query_rows, key_part, preferred_element_type=jnp.float32)
        * score_scale
    )
    allowed_all = allowed[None]
    scores = jnp.where(allowed_all, scores, NEGATIVE)
    highest = jnp.maximum(running, jnp.max(scores, axis=-1))
    factor = jnp.exp(running - highest)
    weights = jnp.where(allowed_all, jnp.exp(scores - highest[..., None]), 0.0)
    denominator = denominator * factor + jnp.sum(weights, axis=-1)
    numerator = numerator * factor[..., None] + jnp.einsum(
        "ptu,ud->ptd",
        weights.astype(jnp.bfloat16),
        value_part,
        preferred_element_type=jnp.float32,
    )
    return (highest, denominator, numerator)


def absorb_tiled(fold_carry, query_rows, key_part, value_part, allowed, score_scale):
    key_count = key_part.shape[0]
    tile_width = math.gcd(key_count, 512)

    def one_tile(tile_index, inner):
        tile_start = tile_index * tile_width
        return absorb(
            inner,
            query_rows,
            lax.dynamic_slice_in_dim(key_part, tile_start, tile_width, 0),
            lax.dynamic_slice_in_dim(value_part, tile_start, tile_width, 0),
            lax.dynamic_slice_in_dim(allowed, tile_start, tile_width, 1),
            score_scale,
        )

    return lax.fori_loop(0, key_count // tile_width, one_tile, fold_carry)


def empty_state(blocks, group_size, rows_all, head_dim):
    return (
        jnp.full((blocks, group_size, rows_all), NEGATIVE, jnp.float32),
        jnp.zeros((blocks, group_size, rows_all), jnp.float32),
        jnp.zeros((blocks, group_size, rows_all, head_dim), jnp.float32),
    )


def absorb_chunk(fold_carry, query_rows, chunk, key_blocks, row_limit, score_scale):
    head_dim = query_rows.shape[-1]
    block_len = chunk.shape[-2]
    chunk = chunk.reshape(-1, 2 * head_dim)
    key_block = jnp.repeat(key_blocks.reshape(-1), block_len)
    allowed = key_block[None, None, :] < row_limit[:, :, None]
    return jax.vmap(absorb, in_axes=(0, 0, None, None, 0, None))(
        fold_carry, query_rows, chunk[:, :head_dim], chunk[:, head_dim:], allowed, score_scale
    )


def merge(first, second):
    high_a, den_a, num_a = first
    high_b, den_b, num_b = second
    highest = jnp.maximum(high_a, high_b)
    factor_a = jnp.exp(high_a - highest)
    factor_b = jnp.exp(high_b - highest)
    return (
        highest,
        den_a * factor_a + den_b * factor_b,
        num_a * factor_a[..., None] + num_b * factor_b[..., None],
    )


def swap(value, axis):
    return lax.ppermute(value, axis, [(0, 1), (1, 0)])


def local(hidden, queries, kv_panel, layout):
    block_len = hidden.shape[2]
    model_width = hidden.shape[3]
    heads_kv = kv_panel.shape[0]
    chunk_rows = kv_panel.shape[1]
    head_dim = kv_panel.shape[2] // 2
    group_size = queries.shape[3] // (heads_kv * head_dim)
    group_width = group_size * head_dim
    score_scale = head_dim ** (-0.5)
    n_chunks = model_width // chunk_rows
    x = lax.axis_index("x")
    y = lax.axis_index("y")
    zh = lax.axis_index("zh")
    core = lax.axis_index("core")
    fsdp = lax.axis_index("fsdp")
    ctx = ((x * 4 + y) * 2 + zh) * 2 + core
    block_table = layout[0]

    z_size = 2 * n_chunks
    forward = [(z, (z + 1) % z_size) for z in range(z_size)]
    backward = [(z, (z - 1) % z_size) for z in range(z_size)]
    mine = lax.dynamic_index_in_dim(kv_panel, core, 0, keepdims=False)
    going_up = mine
    going_down = mine
    from_below = []
    from_above = []
    for step in range(1, n_chunks // 2 + 1):
        going_up = lax.ppermute(going_up, ("zh", "fsdp"), forward)
        from_below.append(going_up)
        if step < n_chunks // 2:
            going_down = lax.ppermute(going_down, ("zh", "fsdp"), backward)
            from_above.append(going_down)
    panel = jnp.concatenate([mine] + from_above + from_below[::-1], axis=0)

    own_rows = hidden.reshape(2, block_len, model_width)
    token_rows = jnp.stack([own_rows, swap(own_rows, "core")])
    token_rows = jnp.roll(token_rows, -fsdp * chunk_rows, axis=-1)
    own_queries = queries.reshape(2, block_len, heads_kv, group_width)
    query_mine = lax.dynamic_index_in_dim(own_queries, core, 2, keepdims=False)
    query_other = lax.dynamic_index_in_dim(own_queries, 1 - core, 2, keepdims=False)
    query_blocks = jnp.stack([query_mine, swap(query_other, "core")])
    ctx_blocks = jnp.stack([ctx, ctx + 1 - 2 * core])
    own_blocks = block_table[ctx_blocks]

    projected = jnp.einsum(
        "bctd,de->bcte", token_rows, panel, preferred_element_type=jnp.float32
    )
    positions = own_blocks[:, None] * block_len + jnp.arange(block_len, dtype=jnp.int32)
    key_rows = rotate_keys(projected[..., :head_dim], positions[:, None, :], head_dim).astype(
        jnp.bfloat16
    )
    value_rows = projected[..., head_dim:].astype(jnp.bfloat16)

    clean = jnp.concatenate([key_rows[:, 0], value_rows[:, 0]], axis=-1)
    rows_all = 2 * block_len
    query_rows = query_blocks.reshape(2, rows_all, group_size, head_dim)
    row_limit = own_blocks[:, None] + jnp.concatenate(
        [jnp.ones((block_len,), jnp.int32), jnp.zeros((block_len,), jnp.int32)]
    )[None, :]
    src_x = jnp.arange(4)
    src_y = jnp.arange(4)
    src_zh = (zh + jnp.arange(2)) % 2
    src_core = (core + jnp.arange(2)) % 2
    src = (
        (src_x[None, None, :, None] * 4 + src_y[None, :, None, None]) * 2
        + src_zh[:, None, None, None]
    ) * 2 + src_core
    every_block = block_table[src.reshape(-1)].reshape(2, 4, 4, 2)

    def chain(rows, side):
        blocks = jnp.swapaxes(every_block[side], 0, 1).reshape(-1, 4, 2)
        spread = jnp.broadcast_to(rows[None], (16,) + rows.shape)
        gathered = lax.all_to_all(spread, ("x", "y"), 0, 0, tiled=True).reshape(-1, 4, *rows.shape)

        def one_part(part, fold_carry):
            return absorb_chunk(
                fold_carry, query_rows,
                lax.dynamic_index_in_dim(gathered, part, 0, keepdims=False),
                lax.dynamic_index_in_dim(blocks, part, 0, keepdims=False),
                row_limit, score_scale,
            )

        fold_carry = empty_state(2, group_size, rows_all, head_dim)
        return lax.fori_loop(0, gathered.shape[0], one_part, fold_carry)

    noisy_ok = jnp.broadcast_to((jnp.arange(rows_all) >= block_len)[:, None], (rows_all, block_len))
    noisy_state = jax.vmap(absorb, in_axes=(0, 0, 0, 0, None, None))(
        empty_state(2, group_size, rows_all, head_dim),
        query_rows, key_rows[:, 1], value_rows[:, 1], noisy_ok, score_scale,
    )
    near = chain(clean, 0)
    far = chain(swap(clean, "zh"), 1)
    highest, denominator, numerator = merge(merge(noisy_state, near), far)
    attended = jnp.transpose(numerator / denominator[..., None], (0, 2, 1, 3))
    attended = attended.astype(jnp.bfloat16).reshape(2, 2, block_len, group_width)
    returned = swap(attended[1], "core")
    first = jnp.where(core == 0, attended[0], returned)
    second = jnp.where(core == 0, returned, attended[0])
    result = jnp.concatenate([first, second], axis=-1)
    return result.reshape(2, 1, block_len, heads_kv * group_width)


def solution(mesh):
    axis_sizes = dict(zip(mesh.axis_names, mesh.devices.shape))
    assert axis_sizes["ctx"] == 64
    fine = Mesh(mesh.devices.reshape(4, 4, 2, 2, axis_sizes["fsdp"]), CTX + ("fsdp",))
    return jax.shard_map(
        local,
        mesh=fine,
        in_specs=(
            P(None, "fsdp", CTX, None),
            P(None, "fsdp", CTX, None),
            P(None, "fsdp", None),
            P("fsdp", None),
        ),
        out_specs=P(None, "fsdp", CTX, None),
        check_vma=False,
    )
```
